768 devices in a mesh: dp: 192 (over y, z, core), tensor: 4 (over x).
Axes of the slice: x: 4, y: 8, z: 12, core: 2. Of those that a mesh axis runs over, the one named last changes fastest.
Arguments:
- inputs: bfloat16 [24576, 4096], P('dp'), may hold values from -6 to 6
- d_hidden: bfloat16 [24576, 14336], P('dp', 'tensor'), may hold values from -6 to 6
- tile_store: bfloat16 [4, 192, 4096], P('tensor', 'dp'), may hold values from -0.4375 to 0.4375
- tile_row: int32 [224, 3], P('tensor'), may hold values from 0 to 63, as said below
- tile_slot: int32 [224, 3], P('tensor'), may hold values from 0 to 191, as said below
Outputs:
- grad_inputs: bfloat16 [24576, 4096], P('dp', 'tensor')
- grad_tiles: float32 [4, 192, 4096], P('tensor', 'dp')
The draws below stay inside these ranges and needn't reach their ends.
Inputs may be any that keep to these rules, and one draw needn't show every extreme that they name: `tile_row`: the 3 tile rows of one tile column are all different. `tile_slot`: tile column c uses the store of index c // (14336 // (64 * 4)) of tensor; the slots of one store are all different; slot s belongs to the owner s // 1 of dp; in every store some owner has all its 1 slots used.
All inputs are finite; a program needn't handle non-finite values.
Results may differ from the reference program's by a relative error of at most 0.012.
Values may be sent and summed in bfloat16 or wider, within the bound.
No kernel may reach another device: no remote copies, remote signals or barrier semaphores. Data moves between devices by JAX's collectives and lax.ppermute only.
A program may use at most 64 MiB of HBM per device.

```python
import jax
import jax.numpy as jnp
from jax import lax

D = 4096
FF = 14336
TILE = 64
KEEP = 3
TOK_DEV = 128
CAP = 1
SLOTS = 192
TOKENS = 24576
N_DP = 192
N_TENSOR = 4


def draw_tile_row(key, part):
    column_count = FF // TILE
    key_list = jax.random.split(key, column_count)

    def one_column(sub_key):
        return jax.random.permutation(sub_key, D // TILE)[:KEEP]
    return jax.vmap(one_column)(key_list).astype(jnp.int32)


def draw_tile_slot(key, part):
    per_slice = FF // TILE // N_TENSOR
    key_list = jax.random.split(jax.random.fold_in(key, 7), N_TENSOR)

    def one_slice(sub_key):
        owner_key, jitter_key = jax.random.split(sub_key)
        full_owner = jax.random.randint(owner_key, (), 0, N_DP)
        jitter_value = jax.random.randint(jitter_key, (SLOTS,), 0, 2 ** 19)
        slot_ids = jnp.arange(SLOTS, dtype=jnp.int32)
        other_owner = (slot_ids // CAP != full_owner).astype(jnp.int32)
        slot_score = jitter_value * SLOTS + slot_ids + other_owner * (2 ** 19 * SLOTS)
        slot_order = jnp.argsort(slot_score, stable=True)
        return slot_order[:per_slice * KEEP].reshape(per_slice, KEEP)
    return jax.vmap(one_slice)(key_list).reshape(per_slice * N_TENSOR, KEEP).astype(jnp.int32)


def block_levels(rng, dims, cuts, smallest, top_value):
    factor_of = 1.0
    for dim, shards_of in cuts:
        draws = jax.random.uniform(jax.random.fold_in(jax.random.fold_in(rng, 6), dim), (shards_of,), jnp.float32, smallest / len(cuts), top_value / len(cuts))
        factor_of = factor_of * jnp.repeat(jnp.exp(draws), dims[dim] // shards_of).reshape((-1,) + (1,) * (len(dims) - 1 - dim))
    return factor_of


def gaussian(own_key, extent, deviation, limit, shards=(), kind=jnp.bfloat16):
    entries = deviation * jax.random.normal(own_key, extent, jnp.float32)
    if shards:
        entries = entries * block_levels(own_key, extent, shards, -0.22, 0.18)
    return jnp.clip(entries, -limit, limit).astype(kind)


def setup_inputs(seed: int = 0) -> dict:
    streams_of = jax.random.split(jax.random.key(seed), 6)
    return {
        "inputs": gaussian(streams_of[0], (TOKENS, D), 1.0, 6.0, ((0, 192),)),
        "d_hidden": gaussian(streams_of[1], (TOKENS, FF), 1.0, 6.0, ((0, 192), (1, 4))),
        "tile_store": gaussian(streams_of[2], (N_TENSOR, SLOTS, TILE * TILE), (KEEP * TILE) ** -0.5, 0.4375, ((0, 4), (1, 192))),
        "tile_row": draw_tile_row(jax.random.fold_in(streams_of[5], 71), 0),
        "tile_slot": draw_tile_slot(jax.random.fold_in(streams_of[5], 71), 0),
    }


def silu_slope(value):
    sigma = jax.nn.sigmoid(value)
    return sigma * (1.0 + value * (1.0 - sigma))


def reference(inputs, d_hidden, tile_store, tile_row, tile_slot):
    column_count = FF // TILE
    per_slice = column_count // N_TENSOR
    row_count = D // TILE
    slice_index = (jnp.arange(column_count, dtype=jnp.int32) // per_slice).astype(jnp.int32)
    kept_tiles = tile_store[slice_index[:, None], tile_slot]
    kept_tiles = kept_tiles.astype(jnp.float32).reshape(column_count, KEEP, TILE, TILE)
    row_ids = jnp.arange(row_count, dtype=jnp.int32)
    row_onehot = (tile_row[:, :, None] == row_ids[None, None, :]).astype(jnp.float32)
    row_onehot = row_onehot.reshape(N_TENSOR, per_slice, KEEP, row_count)
    input_blocks = inputs.reshape(N_DP, TOK_DEV, row_count, TILE)
    grad_blocks = d_hidden.reshape(N_DP, TOK_DEV, column_count, TILE)
    highest = lax.Precision.HIGHEST

    def block_step(grad_total, block_pair):
        input_block, grad_block = block_pair
        picked = input_block[:, tile_row].astype(jnp.float32)
        pre_act = jnp.einsum('tcki,ckij->tcj', picked, kept_tiles, precision=highest)
        pre_grad = (grad_block.astype(jnp.float32) * silu_slope(pre_act)).astype(jnp.bfloat16)
        pre_grad = lax.optimization_barrier(pre_grad).astype(jnp.float32)
        back_part = jnp.einsum('tcj,ckij->tcki', pre_grad, kept_tiles, precision=highest)
        back_part = back_part.reshape(TOK_DEV, N_TENSOR, per_slice, KEEP, TILE)
        partials = jnp.einsum('tscki,sckr->stri', back_part, row_onehot, precision=highest)
        partials = partials.reshape(N_TENSOR, TOK_DEV, D).astype(jnp.bfloat16)
        partials = lax.optimization_barrier(partials).astype(jnp.float32)
        grad_rows = jnp.sum(partials, axis=0).astype(jnp.bfloat16)
        grad_term = jnp.einsum('tcki,tcj->ckij', picked, pre_grad, precision=highest)
        return grad_total + grad_term, grad_rows

    start_total = jnp.zeros((column_count, KEEP, TILE, TILE), jnp.float32)
    grad_total, grad_rows = lax.scan(block_step, start_total, (input_blocks, grad_blocks))
    grad_inputs = grad_rows.reshape(TOKENS, D)
    slot_store = jnp.zeros((N_TENSOR, N_DP * CAP, TILE * TILE), jnp.float32)
    slot_store = slot_store.at[slice_index[:, None], tile_slot].set(grad_total.reshape(column_count, KEEP, TILE * TILE))
    return grad_inputs, slot_store
```

```python
import jax
import jax.numpy as jnp
from jax import lax
from jax.sharding import Mesh
from jax.sharding import PartitionSpec as P

TILE = 64
DP_AXES = ("y", "z", "c")


def silu_slope(value):
    sigma = jax.nn.sigmoid(value)
    return sigma * (1.0 + value * (1.0 - sigma))


def pair_over_core(block, axis):
    core = lax.axis_index("c")
    other = lax.ppermute(block, "c", [(0, 1), (1, 0)])
    first = jnp.where(core == 0, block, other)
    second = jnp.where(core == 0, other, block)
    return jnp.concatenate([first, second], axis=axis)


def gather_by_a2a(block, name, count):
    copies = jnp.broadcast_to(block[None], (count,) + block.shape)
    got = lax.all_to_all(copies, name, 0, 0, tiled=True)
    return got.reshape((count * block.shape[0],) + block.shape[1:])


def reduce_by_a2a(value, name, count):
    parts = value.reshape((count, value.shape[0] // count) + value.shape[1:])
    got = lax.all_to_all(parts, name, 0, 0, tiled=True)
    return got.sum(axis=0)


def make_local(ny, nz, nc, nx):
    def local(inputs, d_hidden, tile_store, tile_row, tile_slot):
        tok_rows = inputs.shape[0]
        model_width = inputs.shape[1]
        row_count = model_width // TILE
        per_slice = tile_row.shape[0]
        keep_count = tile_row.shape[1]
        flat = tile_store.shape[-1]
        own = tile_store.reshape(1, flat)
        chip = pair_over_core(own, 0)
        row_z = gather_by_a2a(chip, "z", nz)
        gathered = gather_by_a2a(row_z, "y", ny)
        slot_count = gathered.shape[0]
        kept_tiles = gathered[tile_slot].reshape(per_slice, keep_count, TILE, TILE)
        input_blocks = inputs.reshape(tok_rows, row_count, TILE)
        picked = input_blocks[:, tile_row]
        pre_act = jnp.einsum("tcki,ckij->tcj", picked, kept_tiles, preferred_element_type=jnp.float32)
        upstream = d_hidden.reshape(tok_rows, per_slice, TILE).astype(jnp.float32)
        pre_grad = (upstream * silu_slope(pre_act)).astype(jnp.bfloat16)
        row_ids = jnp.arange(row_count, dtype=jnp.int32)
        back_all = jnp.einsum(
            "tcj,ckij->tcki", pre_grad, kept_tiles, preferred_element_type=jnp.float32
        )
        row_select = (tile_row[:, :, None] == row_ids[None, None, :]).astype(jnp.float32)
        partial_value = jnp.einsum(
            "tcki,ckr->tri", back_all, row_select, precision=lax.Precision.HIGHEST
        )
        partial_value = partial_value.reshape(tok_rows, model_width).astype(jnp.bfloat16)
        width = model_width // nx
        chunks = partial_value.reshape(tok_rows, nx, width)
        me = lax.axis_index("x")
        acc = lax.dynamic_index_in_dim(chunks, me, axis=1, keepdims=False).astype(jnp.float32)
        for shift in range(1, nx):
            send = lax.dynamic_index_in_dim(chunks, (me + shift) % nx, axis=1, keepdims=False)
            got = lax.ppermute(send, "x", [(j, (j + shift) % nx) for j in range(nx)])
            acc = acc + got.astype(jnp.float32)
        grad_inputs = acc.astype(jnp.bfloat16)
        flat_slot = tile_slot.reshape(-1)
        grad_term = jnp.einsum("tcki,tcj->ckij", picked, pre_grad, preferred_element_type=jnp.float32)
        slot_store = jnp.zeros((slot_count, TILE * TILE), jnp.float32)
        slot_store = slot_store.at[flat_slot].set(
            grad_term.reshape(per_slice * keep_count, TILE * TILE)
        )
        grid = slot_store.reshape(ny, nz, nc, flat)
        core = lax.axis_index("c")
        mine = lax.dynamic_index_in_dim(grid, core, axis=2, keepdims=False)
        theirs = lax.dynamic_index_in_dim(grid, 1 - core, axis=2, keepdims=False)
        chip_sum = mine + lax.ppermute(theirs, "c", [(0, 1), (1, 0)])
        by_z = jnp.swapaxes(chip_sum, 0, 1).reshape(nz * ny, flat)
        row_sum = reduce_by_a2a(by_z, "z", nz)
        owned = reduce_by_a2a(row_sum, "y", ny)
        return (grad_inputs, owned.reshape(1, 1, flat))

    return local


def split_dp(mesh):
    devices = mesh.devices
    column = list(devices[:, 0])
    cores = len({d.core_on_chip for d in column})
    zs = len({d.coords[2] for d in column})
    ys = len(column) // (cores * zs)
    assert ys * zs * cores == len(column) and cores == 2
    return ys, zs, cores


def solution(mesh):
    ny, nz, nc = split_dp(mesh)
    nx = mesh.devices.shape[1]
    grid = Mesh(mesh.devices.reshape(ny, nz, nc, nx), DP_AXES + ("x",))
    placed = (
        P(DP_AXES, None),
        P(DP_AXES, "x"),
        P("x", DP_AXES, None),
        P("x", None),
        P("x", None),
    )
    return jax.shard_map(
        make_local(ny, nz, nc, nx),
        mesh=grid,
        in_specs=placed,
        out_specs=(P(DP_AXES, "x"), P("x", DP_AXES, None)),
        check_vma=False,
    )
```

```python
import jax
import jax.numpy as jnp
from jax import lax
from jax.sharding import Mesh
from jax.sharding import PartitionSpec as P

TILE = 64
DP_AXES = ("y", "z", "c")


def silu_slope(value):
    sigma = jax.nn.sigmoid(value)
    return sigma * (1.0 + value * (1.0 - sigma))


def pair_over_core(block, axis):
    core = lax.axis_index("c")
    other = lax.ppermute(block, "c", [(0, 1), (1, 0)])
    first = jnp.where(core == 0, block, other)
    second = jnp.where(core == 0, other, block)
    return jnp.concatenate([first, second], axis=axis)


def gather_by_a2a(block, name, count):
    copies = jnp.broadcast_to(block[None], (count,) + block.shape)
    got = lax.all_to_all(copies, name, 0, 0, tiled=True)
    return got.reshape((count * block.shape[0],) + block.shape[1:])


def reduce_by_a2a(value, name, count):
    parts = value.reshape((count, value.shape[0] // count) + value.shape[1:])
    got = lax.all_to_all(parts, name, 0, 0, tiled=True)
    return got.sum(axis=0)


def make_local(ny, nz, nc, nx):
    def local(inputs, d_hidden, tile_store, tile_row, tile_slot):
        tok_rows = inputs.shape[0]
        model_width = inputs.shape[1]
        row_count = model_width // TILE
        per_slice = tile_row.shape[0]
        keep_count = tile_row.shape[1]
        cap = tile_store.shape[1]
        flat = tile_store.shape[-1]
        half = ny * nz * cap
        core = lax.axis_index("c")
        owner = tile_slot // cap
        slot_k = tile_slot % cap
        rel_core = (owner % nc + nc - core) % nc
        owner_y = owner // (nz * nc)
        owner_z = (owner // nc) % nz
        rel_slot = ((rel_core * ny + owner_y) * nz + owner_z) * cap + slot_k
        own = tile_store.reshape(cap, flat)
        row_z = gather_by_a2a(own, "z", nz)
        mine_tiles = gather_by_a2a(row_z, "y", ny)
        other_tiles = lax.ppermute(mine_tiles, "c", [(0, 1), (1, 0)])
        gathered = jnp.concatenate([mine_tiles, other_tiles], axis=0)
        kept_tiles = gathered[rel_slot].reshape(per_slice, keep_count, TILE, TILE)
        input_blocks = inputs.reshape(tok_rows, row_count, TILE)
        picked = input_blocks[:, tile_row]
        pre_act = jnp.einsum("tcki,ckij->tcj", picked, kept_tiles, preferred_element_type=jnp.float32)
        upstream = d_hidden.reshape(tok_rows, per_slice, TILE).astype(jnp.float32)
        pre_grad = (upstream * silu_slope(pre_act)).astype(jnp.bfloat16)
        row_ids = jnp.arange(row_count, dtype=jnp.int32)
        back_all = jnp.einsum(
            "tcj,ckij->tcki", pre_grad, kept_tiles, preferred_element_type=jnp.float32
        )
        row_select = (tile_row[:, :, None] == row_ids[None, None, :]).astype(jnp.float32)
        partial_value = jnp.einsum(
            "tcki,ckr->tri", back_all, row_select, precision=lax.Precision.HIGHEST
        )
        partial_value = partial_value.reshape(tok_rows, model_width).astype(jnp.bfloat16)
        width = model_width // nx
        chunks = partial_value.reshape(tok_rows, nx, width)
        me = lax.axis_index("x")
        acc = lax.dynamic_index_in_dim(chunks, me, axis=1, keepdims=False).astype(jnp.float32)
        for shift in range(1, nx):
            send = lax.dynamic_index_in_dim(chunks, (me + shift) % nx, axis=1, keepdims=False)
            got = lax.ppermute(send, "x", [(j, (j + shift) % nx) for j in range(nx)])
            acc = acc + got.astype(jnp.float32)
        grad_inputs = acc.astype(jnp.bfloat16)
        grad_term = jnp.einsum("tcki,tcj->ckij", picked, pre_grad, preferred_element_type=jnp.float32)
        slot_store = jnp.zeros((nc * half, flat), jnp.float32)
        slot_store = slot_store.at[rel_slot.reshape(-1)].set(
            grad_term.reshape(per_slice * keep_count, flat)
        )
        chip_sum = slot_store[:half] + lax.ppermute(slot_store[half:], "c", [(0, 1), (1, 0)])
        by_y = chip_sum.reshape(ny, nz * cap * flat)
        col_sum = reduce_by_a2a(by_y, "y", ny).reshape(nz, cap * flat)
        owned = reduce_by_a2a(col_sum, "z", nz)
        return (grad_inputs, owned.reshape(1, cap, flat))

    return local


def split_dp(mesh):
    devices = mesh.devices
    column = list(devices[:, 0])
    cores = len({d.core_on_chip for d in column})
    zs = len({d.coords[2] for d in column})
    ys = len(column) // (cores * zs)
    assert ys * zs * cores == len(column) and cores == 2
    return ys, zs, cores


def solution(mesh):
    ny, nz, nc = split_dp(mesh)
    nx = mesh.devices.shape[1]
    grid = Mesh(mesh.devices.reshape(ny, nz, nc, nx), DP_AXES + ("x",))
    placed = (
        P(DP_AXES, None),
        P(DP_AXES, "x"),
        P("x", DP_AXES, None),
        P("x", None),
        P("x", None),
    )
    return jax.shard_map(
        make_local(ny, nz, nc, nx),
        mesh=grid,
        in_specs=placed,
        out_specs=(P(DP_AXES, "x"), P("x", DP_AXES, None)),
        check_vma=False,
    )
```

```python
import jax
import jax.numpy as jnp
from jax import lax
from jax.sharding import Mesh
from jax.sharding import PartitionSpec as P

TILE = 64
DP_AXES = ("y", "z", "c")


def silu_slope(value):
    sigma = jax.nn.sigmoid(value)
    return sigma * (1.0 + value * (1.0 - sigma))


def pair_over_core(block, axis):
    core = lax.axis_index("c")
    other = lax.ppermute(block, "c", [(0, 1), (1, 0)])
    first = jnp.where(core == 0, block, other)
    second = jnp.where(core == 0, other, block)
    return jnp.concatenate([first, second], axis=axis)


def gather_by_a2a(block, name, count):
    copies = jnp.broadcast_to(block[None], (count,) + block.shape)
    got = lax.all_to_all(copies, name, 0, 0, tiled=True)
    return got.reshape((count * block.shape[0],) + block.shape[1:])


def reduce_by_a2a(value, name, count):
    parts = value.reshape((count, value.shape[0] // count) + value.shape[1:])
    got = lax.all_to_all(parts, name, 0, 0, tiled=True)
    return got.sum(axis=0)


def make_local(ny, nz, nc, nx):
    def local(inputs, d_hidden, tile_store, tile_row, tile_slot):
        tok_rows = inputs.shape[0]
        model_width = inputs.shape[1]
        row_count = model_width // TILE
        per_slice = tile_row.shape[0]
        keep_count = tile_row.shape[1]
        cap = tile_store.shape[1]
        flat = tile_store.shape[-1]
        half = ny * nz * cap
        core = lax.axis_index("c")
        owner = tile_slot // cap
        slot_k = tile_slot % cap
        rel_core = (owner % nc + nc - core) % nc
        owner_y = owner // (nz * nc)
        owner_z = (owner // nc) % nz
        rel_slot = ((rel_core * ny + owner_y) * nz + owner_z) * cap + slot_k
        own = tile_store.reshape(cap, flat)
        row_z = gather_by_a2a(own, "z", nz)
        mine_tiles = gather_by_a2a(row_z, "y", ny)
        other_tiles = lax.ppermute(mine_tiles, "c", [(0, 1), (1, 0)])
        gathered = jnp.concatenate([mine_tiles, other_tiles], axis=0)
        kept_tiles = gathered[rel_slot].reshape(per_slice, keep_count, TILE, TILE)
        input_blocks = inputs.reshape(tok_rows, row_count, TILE)
        picked = input_blocks[:, tile_row]
        pre_act = jnp.einsum("tcki,ckij->tcj", picked, kept_tiles, preferred_element_type=jnp.float32)
        upstream = d_hidden.reshape(tok_rows, per_slice, TILE).astype(jnp.float32)
        pre_grad = (upstream * silu_slope(pre_act)).astype(jnp.bfloat16)
        row_ids = jnp.arange(row_count, dtype=jnp.int32)
        back_all = jnp.einsum(
            "tcj,ckij->tcki", pre_grad, kept_tiles, preferred_element_type=jnp.float32
        )
        row_select = (tile_row[:, :, None] == row_ids[None, None, :]).astype(jnp.float32)
        partial_value = jnp.einsum(
            "tcki,ckr->tri", back_all, row_select, precision=lax.Precision.HIGHEST
        )
        partial_value = partial_value.reshape(tok_rows, model_width).astype(jnp.bfloat16)
        width = model_width // nx
        chunks = partial_value.reshape(tok_rows, nx, width)
        me = lax.axis_index("x")
        acc = lax.dynamic_index_in_dim(chunks, me, axis=1, keepdims=False).astype(jnp.float32)
        for shift in range(1, nx):
            send = lax.dynamic_index_in_dim(chunks, (me + shift) % nx, axis=1, keepdims=False)
            got = lax.ppermute(send, "x", [(j, (j + shift) % nx) for j in range(nx)])
            acc = acc + got.astype(jnp.float32)
        grad_inputs = acc.astype(jnp.bfloat16)
        grad_term = jnp.einsum("tcki,tcj->ckij", picked, pre_grad, preferred_element_type=jnp.float32)
        lanes = 128
        rows = flat // lanes
        slot_store = jnp.zeros((nc * half, rows, lanes), jnp.float32)
        slot_store = slot_store.at[rel_slot.reshape(-1)].set(
            grad_term.reshape(per_slice * keep_count, rows, lanes)
        )
        chip_sum = slot_store[:half] + lax.ppermute(slot_store[half:], "c", [(0, 1), (1, 0)])
        by_y = chip_sum.reshape(ny, nz * cap * rows, lanes)
        col_sum = reduce_by_a2a(by_y, "y", ny).reshape(nz, cap * rows, lanes)
        owned = reduce_by_a2a(col_sum, "z", nz)
        return (grad_inputs, owned.reshape(1, cap, flat))

    return local


def split_dp(mesh):
    devices = mesh.devices
    column = list(devices[:, 0])
    cores = len({d.core_on_chip for d in column})
    zs = len({d.coords[2] for d in column})
    ys = len(column) // (cores * zs)
    assert ys * zs * cores == len(column) and cores == 2
    return ys, zs, cores


def solution(mesh):
    ny, nz, nc = split_dp(mesh)
    nx = mesh.devices.shape[1]
    grid = Mesh(mesh.devices.reshape(ny, nz, nc, nx), DP_AXES + ("x",))
    placed = (
        P(DP_AXES, None),
        P(DP_AXES, "x"),
        P("x", DP_AXES, None),
        P("x", None),
        P("x", None),
    )
    return jax.shard_map(
        make_local(ny, nz, nc, nx),
        mesh=grid,
        in_specs=placed,
        out_specs=(P(DP_AXES, "x"), P("x", DP_AXES, None)),
        check_vma=False,
    )
```

```python
import jax
import jax.numpy as jnp
from jax import lax
from jax.sharding import Mesh
from jax.sharding import PartitionSpec as P

TILE = 64
DP_AXES = ("y", "z", "c")


def silu_slope(value):
    sigma = jax.nn.sigmoid(value)
    return sigma * (1.0 + value * (1.0 - sigma))


def pair_over_core(block, axis):
    core = lax.axis_index("c")
    other = lax.ppermute(block, "c", [(0, 1), (1, 0)])
    first = jnp.where(core == 0, block, other)
    second = jnp.where(core == 0, other, block)
    return jnp.concatenate([first, second], axis=axis)


def gather_by_a2a(block, name, count):
    copies = jnp.broadcast_to(block[None], (count,) + block.shape)
    got = lax.all_to_all(copies, name, 0, 0, tiled=True)
    return got.reshape((count * block.shape[0],) + block.shape[1:])


def reduce_by_a2a(value, name, count):
    parts = value.reshape((count, value.shape[0] // count) + value.shape[1:])
    got = lax.all_to_all(parts, name, 0, 0, tiled=True)
    return got.sum(axis=0)


def make_local(ny, nz, nc, nx):
    def local(inputs, d_hidden, tile_store, tile_row, tile_slot):
        tok_rows = inputs.shape[0]
        model_width = inputs.shape[1]
        row_count = model_width // TILE
        per_slice = tile_row.shape[0]
        keep_count = tile_row.shape[1]
        cap = tile_store.shape[1]
        flat = tile_store.shape[-1]
        half = ny * nz * cap
        core = lax.axis_index("c")
        owner = tile_slot // cap
        slot_k = tile_slot % cap
        rel_core = (owner % nc + nc - core) % nc
        owner_y = owner // (nz * nc)
        owner_z = (owner // nc) % nz
        rel_slot = ((rel_core * ny + owner_y) * nz + owner_z) * cap + slot_k
        own = tile_store.reshape(cap, flat)
        row_z = gather_by_a2a(own, "z", nz)
        mine_tiles = gather_by_a2a(row_z, "y", ny)
        other_tiles = lax.ppermute(mine_tiles, "c", [(0, 1), (1, 0)])
        gathered = jnp.concatenate([mine_tiles, other_tiles], axis=0)
        kept_tiles = gathered[rel_slot].reshape(per_slice, keep_count, TILE, TILE)
        input_blocks = inputs.reshape(tok_rows, row_count, TILE)
        picked = input_blocks[:, tile_row]
        pre_act = jnp.einsum("tcki,ckij->tcj", picked, kept_tiles, preferred_element_type=jnp.float32)
        upstream = d_hidden.reshape(tok_rows, per_slice, TILE).astype(jnp.float32)
        pre_grad = (upstream * silu_slope(pre_act)).astype(jnp.bfloat16)
        row_ids = jnp.arange(row_count, dtype=jnp.int32)
        back_all = jnp.einsum(
            "tcj,ckij->tcki", pre_grad, kept_tiles, preferred_element_type=jnp.float32
        )
        row_select = (tile_row[:, :, None] == row_ids[None, None, :]).astype(jnp.float32)
        partial_value = jnp.einsum(
            "tcki,ckr->tri", back_all, row_select, precision=lax.Precision.HIGHEST
        )
        partial_value = partial_value.reshape(tok_rows, model_width).astype(jnp.bfloat16)
        width = model_width // nx
        chunks = partial_value.reshape(tok_rows, nx, width)
        me = lax.axis_index("x")
        acc = lax.dynamic_index_in_dim(chunks, me, axis=1, keepdims=False).astype(jnp.float32)
        for shift in range(1, nx):
            send = lax.dynamic_index_in_dim(chunks, (me + shift) % nx, axis=1, keepdims=False)
            got = lax.ppermute(send, "x", [(j, (j + shift) % nx) for j in range(nx)])
            acc = acc + got.astype(jnp.float32)
        grad_inputs = acc.astype(jnp.bfloat16)
        owned_parts = []
        for part in range(2):
            lo = part * (TILE // 2)
            picked_rows = picked[..., lo:lo + TILE // 2]
            grad_term = jnp.einsum(
                "tcki,tcj->ckij", picked_rows, pre_grad, preferred_element_type=jnp.float32
            )
            part_flat = flat // 2
            slot_store = jnp.zeros((nc * half, part_flat), jnp.float32)
            slot_store = slot_store.at[rel_slot.reshape(-1)].set(
                grad_term.reshape(per_slice * keep_count, part_flat)
            )
            chip_sum = slot_store[:half] + lax.ppermute(slot_store[half:], "c", [(0, 1), (1, 0)])
            by_y = chip_sum.reshape(ny, nz * cap * part_flat)
            owned_parts.append(reduce_by_a2a(by_y, "y", ny).reshape(nz, cap, part_flat))
        col_sum = jnp.concatenate(owned_parts, axis=2).reshape(nz, cap * flat)
        owned = reduce_by_a2a(col_sum, "z", nz)
        return (grad_inputs, owned.reshape(1, cap, flat))

    return local


def split_dp(mesh):
    devices = mesh.devices
    column = list(devices[:, 0])
    cores = len({d.core_on_chip for d in column})
    zs = len({d.coords[2] for d in column})
    ys = len(column) // (cores * zs)
    assert ys * zs * cores == len(column) and cores == 2
    return ys, zs, cores


def solution(mesh):
    ny, nz, nc = split_dp(mesh)
    nx = mesh.devices.shape[1]
    grid = Mesh(mesh.devices.reshape(ny, nz, nc, nx), DP_AXES + ("x",))
    placed = (
        P(DP_AXES, None),
        P(DP_AXES, "x"),
        P("x", DP_AXES, None),
        P("x", None),
        P("x", None),
    )
    return jax.shard_map(
        make_local(ny, nz, nc, nx),
        mesh=grid,
        in_specs=placed,
        out_specs=(P(DP_AXES, "x"), P("x", DP_AXES, None)),
        check_vma=False,
    )
```

```python
import jax
import jax.numpy as jnp
from jax import lax
from jax.sharding import Mesh
from jax.sharding import PartitionSpec as P

TILE = 64
DP_AXES = ("y", "z", "c")


def silu_slope(value):
    sigma = jax.nn.sigmoid(value)
    return sigma * (1.0 + value * (1.0 - sigma))


def pair_over_core(block, axis):
    core = lax.axis_index("c")
    other = lax.ppermute(block, "c", [(0, 1), (1, 0)])
    first = jnp.where(core == 0, block, other)
    second = jnp.where(core == 0, other, block)
    return jnp.concatenate([first, second], axis=axis)


def gather_by_a2a(block, name, count):
    copies = jnp.broadcast_to(block[None], (count,) + block.shape)
    got = lax.all_to_all(copies, name, 0, 0, tiled=True)
    return got.reshape((count * block.shape[0],) + block.shape[1:])


def reduce_by_a2a(value, name, count):
    parts = value.reshape((count, value.shape[0] // count) + value.shape[1:])
    got = lax.all_to_all(parts, name, 0, 0, tiled=True)
    return got.sum(axis=0)


def make_local(ny, nz, nc, nx):
    def local(inputs, d_hidden, tile_store, tile_row, tile_slot):
        tok_rows = inputs.shape[0]
        model_width = inputs.shape[1]
        row_count = model_width // TILE
        per_slice = tile_row.shape[0]
        keep_count = tile_row.shape[1]
        cap = tile_store.shape[1]
        flat = tile_store.shape[-1]
        half = ny * nz * cap
        core = lax.axis_index("c")
        owner = tile_slot // cap
        slot_k = tile_slot % cap
        rel_core = (owner % nc + nc - core) % nc
        owner_y = owner // (nz * nc)
        owner_z = (owner // nc) % nz
        rel_slot = ((rel_core * ny + owner_y) * nz + owner_z) * cap + slot_k
        own = tile_store.reshape(cap, flat)
        row_z = gather_by_a2a(own, "z", nz)
        mine_tiles = gather_by_a2a(row_z, "y", ny)
        other_tiles = lax.ppermute(mine_tiles, "c", [(0, 1), (1, 0)])
        gathered = jnp.concatenate([mine_tiles, other_tiles], axis=0)
        kept_tiles = gathered[rel_slot].reshape(per_slice, keep_count, TILE, TILE)
        input_blocks = inputs.reshape(tok_rows, row_count, TILE)
        picked = input_blocks[:, tile_row]
        pre_act = jnp.einsum("tcki,ckij->tcj", picked, kept_tiles, preferred_element_type=jnp.float32)
        upstream = d_hidden.reshape(tok_rows, per_slice, TILE).astype(jnp.float32)
        pre_grad = (upstream * silu_slope(pre_act)).astype(jnp.bfloat16)
        row_ids = jnp.arange(row_count, dtype=jnp.int32)
        back_all = jnp.einsum(
            "tcj,ckij->tcki", pre_grad, kept_tiles, preferred_element_type=jnp.float32
        )
        row_select = (tile_row[:, :, None] == row_ids[None, None, :]).astype(jnp.float32)
        partial_value = jnp.einsum(
            "tcki,ckr->tri", back_all, row_select, precision=lax.Precision.HIGHEST
        )
        partial_value = partial_value.reshape(tok_rows, model_width).astype(jnp.bfloat16)
        width = model_width // nx
        chunks = partial_value.reshape(tok_rows, nx, width)
        me = lax.axis_index("x")
        acc = lax.dynamic_index_in_dim(chunks, me, axis=1, keepdims=False).astype(jnp.float32)
        for shift in range(1, nx):
            send = lax.dynamic_index_in_dim(chunks, (me + shift) % nx, axis=1, keepdims=False)
            got = lax.ppermute(send, "x", [(j, (j + shift) % nx) for j in range(nx)])
            acc = acc + got.astype(jnp.float32)
        grad_inputs = acc.astype(jnp.bfloat16)
        grad_term = jnp.einsum("tcki,tcj->ckij", picked, pre_grad, preferred_element_type=jnp.float32)
        slot_store = jnp.zeros((nc * half, flat), jnp.float32)
        slot_store = slot_store.at[rel_slot.reshape(-1)].set(
            grad_term.reshape(per_slice * keep_count, flat)
        )
        chip_sum = slot_store[:half] + lax.ppermute(slot_store[half:], "c", [(0, 1), (1, 0)])
        by_y = chip_sum.reshape(ny, nz * cap * flat)
        col_sum = reduce_by_a2a(by_y, "y", ny).reshape(nz, cap * flat)
        col_sum, grad_inputs = lax.optimization_barrier((col_sum, grad_inputs))
        owned = reduce_by_a2a(col_sum, "z", nz)
        return (grad_inputs, owned.reshape(1, cap, flat))

    return local


def split_dp(mesh):
    devices = mesh.devices
    column = list(devices[:, 0])
    cores = len({d.core_on_chip for d in column})
    zs = len({d.coords[2] for d in column})
    ys = len(column) // (cores * zs)
    assert ys * zs * cores == len(column) and cores == 2
    return ys, zs, cores


def solution(mesh):
    ny, nz, nc = split_dp(mesh)
    nx = mesh.devices.shape[1]
    grid = Mesh(mesh.devices.reshape(ny, nz, nc, nx), DP_AXES + ("x",))
    placed = (
        P(DP_AXES, None),
        P(DP_AXES, "x"),
        P("x", DP_AXES, None),
        P("x", None),
        P("x", None),
    )
    return jax.shard_map(
        make_local(ny, nz, nc, nx),
        mesh=grid,
        in_specs=placed,
        out_specs=(P(DP_AXES, "x"), P("x", DP_AXES, None)),
        check_vma=False,
    )
```

```python
import jax
import jax.numpy as jnp
from jax import lax
from jax.sharding import Mesh
from jax.sharding import PartitionSpec as P

TILE = 64
DP_AXES = ("y", "z", "c")


def silu_slope(value):
    sigma = jax.nn.sigmoid(value)
    return sigma * (1.0 + value * (1.0 - sigma))


def pair_over_core(block, axis):
    core = lax.axis_index("c")
    other = lax.ppermute(block, "c", [(0, 1), (1, 0)])
    first = jnp.where(core == 0, block, other)
    second = jnp.where(core == 0, other, block)
    return jnp.concatenate([first, second], axis=axis)


def gather_by_a2a(block, name, count):
    copies = jnp.broadcast_to(block[None], (count,) + block.shape)
    got = lax.all_to_all(copies, name, 0, 0, tiled=True)
    return got.reshape((count * block.shape[0],) + block.shape[1:])


def reduce_by_a2a(value, name, count):
    parts = value.reshape((count, value.shape[0] // count) + value.shape[1:])
    got = lax.all_to_all(parts, name, 0, 0, tiled=True)
    return got.sum(axis=0)


def make_local(ny, nz, nc, nx):
    def local(inputs, d_hidden, tile_store, tile_row, tile_slot):
        tok_rows = inputs.shape[0]
        model_width = inputs.shape[1]
        row_count = model_width // TILE
        per_slice = tile_row.shape[0]
        keep_count = tile_row.shape[1]
        cap = tile_store.shape[1]
        flat = tile_store.shape[-1]
        half = ny * nz * cap
        core = lax.axis_index("c")
        owner = tile_slot // cap
        slot_k = tile_slot % cap
        rel_core = (owner % nc + nc - core) % nc
        owner_y = owner // (nz * nc)
        owner_z = (owner // nc) % nz
        rel_slot = ((rel_core * ny + owner_y) * nz + owner_z) * cap + slot_k
        own = tile_store.reshape(cap, flat)
        row_z = gather_by_a2a(own, "z", nz)
        mine_tiles = gather_by_a2a(row_z, "y", ny)
        other_tiles = lax.ppermute(mine_tiles, "c", [(0, 1), (1, 0)])
        gathered = jnp.concatenate([mine_tiles, other_tiles], axis=0)
        kept_tiles = gathered[rel_slot].reshape(per_slice, keep_count, TILE, TILE)
        input_blocks = inputs.reshape(tok_rows, row_count, TILE)
        picked = input_blocks[:, tile_row]
        pre_act = jnp.einsum("tcki,ckij->tcj", picked, kept_tiles, preferred_element_type=jnp.float32)
        upstream = d_hidden.reshape(tok_rows, per_slice, TILE).astype(jnp.float32)
        pre_grad = (upstream * silu_slope(pre_act)).astype(jnp.bfloat16)
        row_ids = jnp.arange(row_count, dtype=jnp.int32)
        back_all = jnp.einsum(
            "tcj,ckij->tcki", pre_grad, kept_tiles, preferred_element_type=jnp.float32
        )
        row_select = (tile_row[:, :, None] == row_ids[None, None, :]).astype(jnp.float32)
        partial_value = jnp.einsum(
            "tcki,ckr->tri", back_all, row_select, precision=lax.Precision.HIGHEST
        )
        partial_value = partial_value.reshape(tok_rows, model_width).astype(jnp.bfloat16)
        width = model_width // nx
        chunks = partial_value.reshape(tok_rows, nx, width)
        me = lax.axis_index("x")
        acc = lax.dynamic_index_in_dim(chunks, me, axis=1, keepdims=False).astype(jnp.float32)
        for shift in range(1, nx):
            send = lax.dynamic_index_in_dim(chunks, (me + shift) % nx, axis=1, keepdims=False)
            got = lax.ppermute(send, "x", [(j, (j + shift) % nx) for j in range(nx)])
            acc = acc + got.astype(jnp.float32)
        grad_inputs = acc.astype(jnp.bfloat16)
        grad_term = jnp.einsum("tcki,tcj->ckij", picked, pre_grad, preferred_element_type=jnp.float32)
        grad_rows = grad_term.reshape(per_slice * keep_count, flat)
        flat_slot = rel_slot.reshape(-1)
        to_partner = flat_slot >= half
        partner_slot = jnp.where(to_partner, flat_slot - half, half)
        own_slot = jnp.where(to_partner, half, flat_slot)
        partner_store = jnp.zeros((half, flat), jnp.float32).at[partner_slot].set(grad_rows, mode="drop")
        arrived = lax.ppermute(partner_store, "c", [(0, 1), (1, 0)])
        own_store = jnp.zeros((half, flat), jnp.float32).at[own_slot].set(grad_rows, mode="drop")
        chip_sum = own_store + arrived
        by_y = chip_sum.reshape(ny, nz * cap * flat)
        col_sum = reduce_by_a2a(by_y, "y", ny).reshape(nz, cap * flat)
        col_sum, grad_inputs = lax.optimization_barrier((col_sum, grad_inputs))
        owned = reduce_by_a2a(col_sum, "z", nz)
        return (grad_inputs, owned.reshape(1, cap, flat))

    return local


def split_dp(mesh):
    devices = mesh.devices
    column = list(devices[:, 0])
    cores = len({d.core_on_chip for d in column})
    zs = len({d.coords[2] for d in column})
    ys = len(column) // (cores * zs)
    assert ys * zs * cores == len(column) and cores == 2
    return ys, zs, cores


def solution(mesh):
    ny, nz, nc = split_dp(mesh)
    nx = mesh.devices.shape[1]
    grid = Mesh(mesh.devices.reshape(ny, nz, nc, nx), DP_AXES + ("x",))
    placed = (
        P(DP_AXES, None),
        P(DP_AXES, "x"),
        P("x", DP_AXES, None),
        P("x", None),
        P("x", None),
    )
    return jax.shard_map(
        make_local(ny, nz, nc, nx),
        mesh=grid,
        in_specs=placed,
        out_specs=(P(DP_AXES, "x"), P("x", DP_AXES, None)),
        check_vma=False,
    )
```

```python
import jax
import jax.numpy as jnp
from jax import lax
from jax.sharding import Mesh
from jax.sharding import PartitionSpec as P

TILE = 64
DP_AXES = ("y", "z", "c")


def silu_slope(value):
    sigma = jax.nn.sigmoid(value)
    return sigma * (1.0 + value * (1.0 - sigma))


def pair_over_core(block, axis):
    core = lax.axis_index("c")
    other = lax.ppermute(block, "c", [(0, 1), (1, 0)])
    first = jnp.where(core == 0, block, other)
    second = jnp.where(core == 0, other, block)
    return jnp.concatenate([first, second], axis=axis)


def gather_by_a2a(block, name, count):
    copies = jnp.broadcast_to(block[None], (count,) + block.shape)
    got = lax.all_to_all(copies, name, 0, 0, tiled=True)
    return got.reshape((count * block.shape[0],) + block.shape[1:])


def reduce_by_a2a(value, name, count):
    parts = value.reshape((count, value.shape[0] // count) + value.shape[1:])
    got = lax.all_to_all(parts, name, 0, 0, tiled=True)
    return got.sum(axis=0)


def make_local(ny, nz, nc, nx):
    def local(inputs, d_hidden, tile_store, tile_row, tile_slot):
        tok_rows = inputs.shape[0]
        model_width = inputs.shape[1]
        row_count = model_width // TILE
        per_slice = tile_row.shape[0]
        keep_count = tile_row.shape[1]
        cap = tile_store.shape[1]
        flat = tile_store.shape[-1]
        half = ny * nz * cap
        core = lax.axis_index("c")
        owner = tile_slot // cap
        slot_k = tile_slot % cap
        rel_core = (owner % nc + nc - core) % nc
        owner_y = owner // (nz * nc)
        owner_z = (owner // nc) % nz
        rel_slot = ((rel_core * ny + owner_y) * nz + owner_z) * cap + slot_k
        own = tile_store.reshape(cap, flat)
        row_z = gather_by_a2a(own, "z", nz)
        mine_tiles = gather_by_a2a(row_z, "y", ny)
        input_blocks = inputs.reshape(tok_rows, row_count, TILE)
        picked = input_blocks[:, tile_row]
        upstream = d_hidden.reshape(tok_rows, per_slice, TILE).astype(jnp.float32)
        mine_tiles, picked, upstream, rel_slot = lax.optimization_barrier(
            (mine_tiles, picked, upstream, rel_slot)
        )
        other_tiles = lax.ppermute(mine_tiles, "c", [(0, 1), (1, 0)])
        gathered = jnp.concatenate([mine_tiles, other_tiles], axis=0)
        kept_tiles = gathered[rel_slot].reshape(per_slice, keep_count, TILE, TILE)
        pre_act = jnp.einsum("tcki,ckij->tcj", picked, kept_tiles, preferred_element_type=jnp.float32)
        pre_grad = (upstream * silu_slope(pre_act)).astype(jnp.bfloat16)
        row_ids = jnp.arange(row_count, dtype=jnp.int32)
        back_all = jnp.einsum(
            "tcj,ckij->tcki", pre_grad, kept_tiles, preferred_element_type=jnp.float32
        )
        row_select = (tile_row[:, :, None] == row_ids[None, None, :]).astype(jnp.float32)
        partial_value = jnp.einsum(
            "tcki,ckr->tri", back_all, row_select, precision=lax.Precision.HIGHEST
        )
        partial_value = partial_value.reshape(tok_rows, model_width).astype(jnp.bfloat16)
        width = model_width // nx
        chunks = partial_value.reshape(tok_rows, nx, width)
        me = lax.axis_index("x")
        acc = lax.dynamic_index_in_dim(chunks, me, axis=1, keepdims=False).astype(jnp.float32)
        for shift in range(1, nx):
            send = lax.dynamic_index_in_dim(chunks, (me + shift) % nx, axis=1, keepdims=False)
            got = lax.ppermute(send, "x", [(j, (j + shift) % nx) for j in range(nx)])
            acc = acc + got.astype(jnp.float32)
        grad_inputs = acc.astype(jnp.bfloat16)
        grad_term = jnp.einsum("tcki,tcj->ckij", picked, pre_grad, preferred_element_type=jnp.float32)
        grad_rows = grad_term.reshape(per_slice * keep_count, flat)
        flat_slot = rel_slot.reshape(-1)
        to_partner = flat_slot >= half
        partner_slot = jnp.where(to_partner, flat_slot - half, half)
        own_slot = jnp.where(to_partner, half, flat_slot)
        partner_store = jnp.zeros((half, flat), jnp.float32).at[partner_slot].set(grad_rows, mode="drop")
        arrived = lax.ppermute(partner_store, "c", [(0, 1), (1, 0)])
        own_store = jnp.zeros((half, flat), jnp.float32).at[own_slot].set(grad_rows, mode="drop")
        chip_sum = own_store + arrived
        by_y = chip_sum.reshape(ny, nz * cap * flat)
        col_sum = reduce_by_a2a(by_y, "y", ny).reshape(nz, cap * flat)
        col_sum, grad_inputs = lax.optimization_barrier((col_sum, grad_inputs))
        owned = reduce_by_a2a(col_sum, "z", nz)
        return (grad_inputs, owned.reshape(1, cap, flat))

    return local


def split_dp(mesh):
    devices = mesh.devices
    column = list(devices[:, 0])
    cores = len({d.core_on_chip for d in column})
    zs = len({d.coords[2] for d in column})
    ys = len(column) // (cores * zs)
    assert ys * zs * cores == len(column) and cores == 2
    return ys, zs, cores


def solution(mesh):
    ny, nz, nc = split_dp(mesh)
    nx = mesh.devices.shape[1]
    grid = Mesh(mesh.devices.reshape(ny, nz, nc, nx), DP_AXES + ("x",))
    placed = (
        P(DP_AXES, None),
        P(DP_AXES, "x"),
        P("x", DP_AXES, None),
        P("x", None),
        P("x", None),
    )
    return jax.shard_map(
        make_local(ny, nz, nc, nx),
        mesh=grid,
        in_specs=placed,
        out_specs=(P(DP_AXES, "x"), P("x", DP_AXES, None)),
        check_vma=False,
    )
```

```python
import jax
import jax.numpy as jnp
from jax import lax
from jax.sharding import Mesh
from jax.sharding import PartitionSpec as P

TILE = 64
DP_AXES = ("y", "z", "c")


def silu_slope(value):
    sigma = jax.nn.sigmoid(value)
    return sigma * (1.0 + value * (1.0 - sigma))


def pair_over_core(block, axis):
    core = lax.axis_index("c")
    other = lax.ppermute(block, "c", [(0, 1), (1, 0)])
    first = jnp.where(core == 0, block, other)
    second = jnp.where(core == 0, other, block)
    return jnp.concatenate([first, second], axis=axis)


def gather_by_a2a(block, name, count):
    copies = jnp.broadcast_to(block[None], (count,) + block.shape)
    got = lax.all_to_all(copies, name, 0, 0, tiled=True)
    return got.reshape((count * block.shape[0],) + block.shape[1:])


def reduce_by_a2a(value, name, count):
    parts = value.reshape((count, value.shape[0] // count) + value.shape[1:])
    got = lax.all_to_all(parts, name, 0, 0, tiled=True)
    return got.sum(axis=0)


def make_local(ny, nz, nc, nx):
    def local(inputs, d_hidden, tile_store, tile_row, tile_slot):
        tok_rows = inputs.shape[0]
        model_width = inputs.shape[1]
        row_count = model_width // TILE
        per_slice = tile_row.shape[0]
        keep_count = tile_row.shape[1]
        cap = tile_store.shape[1]
        flat = tile_store.shape[-1]
        half = ny * nz * cap
        core = lax.axis_index("c")
        owner = tile_slot // cap
        slot_k = tile_slot % cap
        rel_core = (owner % nc + nc - core) % nc
        owner_y = owner // (nz * nc)
        owner_z = (owner // nc) % nz
        rel_slot = ((rel_core * ny + owner_y) * nz + owner_z) * cap + slot_k
        own = tile_store.reshape(cap, flat)
        row_z = gather_by_a2a(own, "z", nz)
        mine_tiles = gather_by_a2a(row_z, "y", ny)
        input_blocks = inputs.reshape(tok_rows, row_count, TILE)
        picked = input_blocks[:, tile_row]
        upstream = d_hidden.reshape(tok_rows, per_slice, TILE).astype(jnp.float32)
        mine_tiles, picked, upstream, rel_slot = lax.optimization_barrier(
            (mine_tiles, picked, upstream, rel_slot)
        )
        other_tiles = lax.ppermute(mine_tiles, "c", [(0, 1), (1, 0)])
        local_slot = rel_slot % half
        from_mine = mine_tiles[local_slot]
        from_other = other_tiles[local_slot]
        picked_tiles = jnp.where((rel_slot < half)[..., None], from_mine, from_other)
        kept_tiles = picked_tiles.reshape(per_slice, keep_count, TILE, TILE)
        pre_act = jnp.einsum("tcki,ckij->tcj", picked, kept_tiles, preferred_element_type=jnp.float32)
        pre_grad = (upstream * silu_slope(pre_act)).astype(jnp.bfloat16)
        row_ids = jnp.arange(row_count, dtype=jnp.int32)
        back_all = jnp.einsum(
            "tcj,ckij->tcki", pre_grad, kept_tiles, preferred_element_type=jnp.float32
        )
        row_select = (tile_row[:, :, None] == row_ids[None, None, :]).astype(jnp.float32)
        partial_value = jnp.einsum(
            "tcki,ckr->tri", back_all, row_select, precision=lax.Precision.HIGHEST
        )
        partial_value = partial_value.reshape(tok_rows, model_width).astype(jnp.bfloat16)
        width = model_width // nx
        chunks = partial_value.reshape(tok_rows, nx, width)
        me = lax.axis_index("x")
        acc = lax.dynamic_index_in_dim(chunks, me, axis=1, keepdims=False).astype(jnp.float32)
        for shift in range(1, nx):
            send = lax.dynamic_index_in_dim(chunks, (me + shift) % nx, axis=1, keepdims=False)
            got = lax.ppermute(send, "x", [(j, (j + shift) % nx) for j in range(nx)])
            acc = acc + got.astype(jnp.float32)
        grad_inputs = acc.astype(jnp.bfloat16)
        grad_term = jnp.einsum("tcki,tcj->ckij", picked, pre_grad, preferred_element_type=jnp.float32)
        grad_rows = grad_term.reshape(per_slice * keep_count, flat)
        flat_slot = rel_slot.reshape(-1)
        to_partner = flat_slot >= half
        partner_slot = jnp.where(to_partner, flat_slot - half, half)
        own_slot = jnp.where(to_partner, half, flat_slot)
        partner_store = jnp.zeros((half, flat), jnp.float32).at[partner_slot].set(grad_rows, mode="drop")
        arrived = lax.ppermute(partner_store, "c", [(0, 1), (1, 0)])
        own_store = jnp.zeros((half, flat), jnp.float32).at[own_slot].set(grad_rows, mode="drop")
        chip_sum = own_store + arrived
        by_y = chip_sum.reshape(ny, nz * cap * flat)
        col_sum = reduce_by_a2a(by_y, "y", ny).reshape(nz, cap * flat)
        col_sum, grad_inputs = lax.optimization_barrier((col_sum, grad_inputs))
        owned = reduce_by_a2a(col_sum, "z", nz)
        return (grad_inputs, owned.reshape(1, cap, flat))

    return local


def split_dp(mesh):
    devices = mesh.devices
    column = list(devices[:, 0])
    cores = len({d.core_on_chip for d in column})
    zs = len({d.coords[2] for d in column})
    ys = len(column) // (cores * zs)
    assert ys * zs * cores == len(column) and cores == 2
    return ys, zs, cores


def solution(mesh):
    ny, nz, nc = split_dp(mesh)
    nx = mesh.devices.shape[1]
    grid = Mesh(mesh.devices.reshape(ny, nz, nc, nx), DP_AXES + ("x",))
    placed = (
        P(DP_AXES, None),
        P(DP_AXES, "x"),
        P("x", DP_AXES, None),
        P("x", None),
        P("x", None),
    )
    return jax.shard_map(
        make_local(ny, nz, nc, nx),
        mesh=grid,
        in_specs=placed,
        out_specs=(P(DP_AXES, "x"), P("x", DP_AXES, None)),
        check_vma=False,
    )
```
